256 devices in a mesh: row: 32 (over z, y_hi, core), col: 8 (over y_lo, x).
Axes of the slice: x: 4, y: 4 (y_hi: 2, y_lo: 2; y = y_hi * 2 + y_lo), z: 8, core: 2. Of those that a mesh axis runs over, the one named last changes fastest.
Arguments:
- factor: float32 [49152, 8192], P('row', 'col'), may hold values from -0.0546875 to 0.0546875
- covariance: float32 [49152, 2048], P('row', 'col'), may hold values from -6 to 6
- inv_diagonal: float32 [8192], P(('col', 'row')), may hold values from 0.5 to 4
- columns: int32 [2048], replicated, may hold values from 0 to 8191
Outputs:
- sigma_window: float32 [8192, 2048], P(('col', 'row'))
The draws below stay inside these ranges and needn't reach their ends.
Inputs may be any that keep to these rules, and one draw needn't show every extreme that they name: `columns`: each entry is a separator index; entries may repeat.
All inputs are finite; a program needn't handle non-finite values.
Results may differ from the reference program's by a relative error of at most 0.000071.
Values sent between devices are 32-bit elements; how exact they have to be, the bound alone decides.
No kernel may reach another device: no remote copies, remote signals or barrier semaphores. Data moves between devices by JAX's collectives and lax.ppermute only.
A program may use at most 128 MiB of HBM per device.

```python
import math
import jax
import jax.numpy as jnp
from jax import lax

S = 8192
A = 49152
W = 2048


def with_ends(array, rng, smallest, top_value):
    dims = array.shape
    index_at = [jax.random.randint(jax.random.fold_in(rng, axis), (), 0, dims[axis]) for axis in range(len(dims))]
    array = array.at[tuple(index_at)].set(smallest)
    longest = dims.index(max(dims))
    index_at[longest] = (index_at[longest] + 1) % dims[longest]
    return array.at[tuple(index_at)].set(top_value)


def with_spikes(entries, key, source, target, parts, factor):
    owner, partner = [(jnp.arange(entries.shape[position]) // (entries.shape[position] // parts)).reshape([-1 if axis == position else 1 for axis in range(entries.ndim)]) for position in (source, target)]
    chosen = jax.random.permutation(key, parts)[partner]
    strong = (owner == chosen) | (owner == (partner + parts // 2) % parts)
    return jnp.where(strong, factor * entries, entries)


def steps_of(rng, dims, split, low, largest):
    def one(position, blocks):
        heights = jax.random.uniform(jax.random.fold_in(jax.random.fold_in(rng, 6), position), (blocks,), jnp.float32, low / len(split), largest / len(split))
        return jnp.repeat(jnp.exp(heights), dims[position] // blocks).reshape((-1,) + (1,) * (len(dims) - position - 1))

    gain = one(*split[0])
    for cut in split[1:]:
        gain = gain * one(*cut)
    return gain


def gaussian(own_key, shape, scale, limit, split=(), kind=jnp.bfloat16):
    entries = scale * jax.random.normal(own_key, shape, jnp.float32)
    if split:
        entries = entries * steps_of(own_key, shape, split, -0.22, 0.18)
    return jnp.clip(entries, -limit, limit).astype(kind)


def heavy_noise(own_key, extent, deviation, reach, pieces, heavy, held_as=jnp.bfloat16):
    array = deviation * jax.random.normal(own_key, extent, jnp.float32)
    if pieces:
        array = array * steps_of(own_key, extent, pieces, -0.22, 0.18)
    return jnp.clip(with_spikes(array, jax.random.fold_in(own_key, 3), *heavy), -reach, reach).astype(held_as)


def setup_inputs(seed: int = 0) -> dict:
    arg_keys = jax.random.split(jax.random.key(seed), 5)
    return {
        "factor": heavy_noise(arg_keys[0], (A, S), A ** -0.5, 0.0546875, ((0, 32), (1, 8)), (0, 1, 32, 2.75), jnp.float32),
        "covariance": gaussian(arg_keys[1], (A, W), 1.0, 6.0, ((0, 32), (1, 8)), jnp.float32),
        "inv_diagonal": jnp.clip(jnp.exp(math.log(4.0) - 2.0794415 * jax.random.uniform(arg_keys[2], (S,), jnp.float32) ** steps_of(arg_keys[2], (S,), ((0, 256),), -0.2, 0.2)), 0.5, 4.0),
        "columns": with_ends(jax.random.randint(arg_keys[3], (W,), 0, S), jax.random.fold_in(arg_keys[3], 1), 0, S - 1).astype(jnp.int32),
    }


def reference(factor, covariance, inv_diagonal, columns):
    product = lax.dot_general(factor, covariance, (((0,), (0,)), ((), ())), precision=lax.Precision.HIGHEST, preferred_element_type=jnp.float32)
    row_ids = lax.iota(jnp.int32, inv_diagonal.shape[0])
    on_diagonal = row_ids[:, None] == columns[None, :]
    return jnp.where(on_diagonal, inv_diagonal[:, None], jnp.zeros((), jnp.float32)) - product
```

```python
import jax
import jax.numpy as jnp
from jax import lax
from jax.sharding import Mesh
from jax.sharding import PartitionSpec as P

ROW = ("z", "yh", "core")
COL = ("yl", "x")
SWAP = [(0, 1), (1, 0)]


def shift_x(step):
    return [(i, (i + step) % 4) for i in range(4)]


def contract_rows(left_block, right_block):
    return lax.dot_general(
        left_block,
        right_block,
        (((0,), (0,)), ((), ())),
        precision=lax.Precision.HIGHEST,
        preferred_element_type=jnp.float32,
    )


def gather_columns(cov):
    h0, h1 = cov[:, :128], cov[:, 128:]
    h0_y = lax.ppermute(h0, "yl", SWAP)
    h1_m = lax.ppermute(h1, "x", shift_x(1))
    h1_p = lax.ppermute(h1, "x", shift_x(-1))
    pair = jnp.concatenate([h0, h0_y], axis=1)
    pair_m = lax.ppermute(pair, "x", shift_x(1))
    pair_p = lax.ppermute(pair, "x", shift_x(-1))
    h1_fa = lax.ppermute(h1_m[:, :64], "x", shift_x(1))
    h1_fb = lax.ppermute(h1_p[:, 64:], "x", shift_x(-1))
    h1_y = lax.ppermute(jnp.concatenate([h1, h1_m, h1_p], axis=1), "yl", SWAP)
    pair_fa = lax.ppermute(pair_m[:, :128], "x", shift_x(1))
    pair_fb = lax.ppermute(pair_p[:, 128:], "x", shift_x(-1))
    h1_far = jnp.concatenate([h1_fa, h1_fb], axis=1)
    h1_far_y = lax.ppermute(h1_far, "yl", SWAP)
    return [
        h0, h1,
        pair_p[:, :128], h1_p,
        pair_fa, h1_far,
        pair_m[:, :128], h1_m,
        h0_y, h1_y[:, :128],
        pair_p[:, 128:], h1_y[:, 256:],
        pair_fb, h1_far_y,
        pair_m[:, 128:], h1_y[:, 128:256],
    ]


def pick(blocks, index):
    return lax.dynamic_index_in_dim(blocks, index, axis=1, keepdims=False)


def reduce_rows(partial):
    width = partial.shape[1]
    core = lax.axis_index("core")
    halves = partial.reshape(16, 2, 32, width)
    kept = pick(halves, core) + lax.ppermute(pick(halves, 1 - core), "core", SWAP)
    kept = ring_reduce(kept.reshape(8, 64, width), "z")
    yh = lax.axis_index("yh")
    pairs = kept.reshape(2, 32, width)
    own = lax.dynamic_index_in_dim(pairs, yh, axis=0, keepdims=False)
    other = lax.dynamic_index_in_dim(pairs, 1 - yh, axis=0, keepdims=False)
    return own + lax.ppermute(other, "yh", SWAP)


def ring_reduce(blocks, axis):
    n = blocks.shape[0]
    me = lax.axis_index(axis)
    half = blocks.shape[2] // 2
    fwd, bwd = blocks[:, :, :half], blocks[:, :, half:]
    up = [(i, (i + 1) % n) for i in range(n)]
    down = [(i, (i - 1) % n) for i in range(n)]
    take = lambda b, k: lax.dynamic_index_in_dim(b, k % n, axis=0, keepdims=False)
    acc_f = take(fwd, me + n - 1)
    acc_b = take(bwd, me + 1)
    for step in range(n - 1):
        acc_f = lax.ppermute(acc_f, axis, up) + take(fwd, me + 2 * n - step - 2)
        acc_b = lax.ppermute(acc_b, axis, down) + take(bwd, me + step + 2)
    return jnp.concatenate([acc_f, acc_b], axis=1)


def per_device(factor, covariance, inv_diagonal, columns):
    pieces = gather_columns(covariance)
    product = jnp.concatenate([contract_rows(factor, p) for p in pieces], axis=1)
    reduced = reduce_rows(product)
    rows = reduced.shape[0]
    yl, x = lax.axis_index("yl"), lax.axis_index("x")
    blocks = reduced.reshape(rows, 2, 4, -1)
    blocks = jnp.where(yl == 1, blocks[:, ::-1], blocks)
    blocks = jnp.roll(blocks, x, axis=2)
    reduced = blocks.reshape(rows, -1)
    row_index = (lax.axis_index("z") * 2 + lax.axis_index("yh")) * 2 + lax.axis_index("core")
    block_index = (yl * 4 + x) * 32 + row_index
    row_ids = block_index * rows + lax.iota(jnp.int32, rows)
    on_diagonal = row_ids[:, None] == columns[None, :]
    return jnp.where(on_diagonal, inv_diagonal[:, None], jnp.zeros((), jnp.float32)) - reduced


def solution(mesh):
    devices = mesh.devices.reshape(8, 2, 2, 2, 4)
    fine = Mesh(devices, ("z", "yh", "core", "yl", "x"))
    return jax.shard_map(
        per_device,
        mesh=fine,
        in_specs=(P(ROW, COL), P(ROW, COL), P(COL + ROW), P()),
        out_specs=P(COL + ROW, None),
        check_vma=False,
    )
```

```python
import jax
import jax.numpy as jnp
from jax import lax
from jax.sharding import Mesh
from jax.sharding import PartitionSpec as P

ROW = ("z", "yh", "core")
COL = ("yl", "x")
SWAP = [(0, 1), (1, 0)]


def shift_x(step):
    return [(i, (i + step) % 4) for i in range(4)]


def contract_rows(left_block, right_block):
    return lax.dot_general(
        left_block,
        right_block,
        (((0,), (0,)), ((), ())),
        precision=lax.Precision.HIGHEST,
        preferred_element_type=jnp.float32,
    )


def gather_columns(cov):
    h0, h1 = cov[:, :128], cov[:, 128:]
    h0_y = lax.ppermute(h0, "yl", SWAP)
    h1_m = lax.ppermute(h1, "x", shift_x(1))
    h1_p = lax.ppermute(h1, "x", shift_x(-1))
    pair = jnp.concatenate([h0, h0_y], axis=1)
    pair_m = lax.ppermute(pair, "x", shift_x(1))
    pair_p = lax.ppermute(pair, "x", shift_x(-1))
    h1_fa = lax.ppermute(h1_m[:, :64], "x", shift_x(1))
    h1_fb = lax.ppermute(h1_p[:, 64:], "x", shift_x(-1))
    h1_y = lax.ppermute(jnp.concatenate([h1, h1_m, h1_p], axis=1), "yl", SWAP)
    pair_fa = lax.ppermute(pair_m[:, :128], "x", shift_x(1))
    pair_fb = lax.ppermute(pair_p[:, 128:], "x", shift_x(-1))
    h1_far = jnp.concatenate([h1_fa, h1_fb], axis=1)
    h1_far_y = lax.ppermute(h1_far, "yl", SWAP)
    groups = [
        [cov],
        [h0_y, h1_m, h1_p],
        [pair_m, pair_p, h1_far, h1_y],
        [pair_fa, pair_fb, h1_far_y],
    ]
    tags = [
        (0, 0, 0), (0, 0, 1),
        (1, 0, 0), (0, 3, 1), (0, 1, 1),
        (0, 3, 0), (1, 3, 0), (0, 1, 0), (1, 1, 0), (0, 2, 1), (1, 0, 1), (1, 3, 1), (1, 1, 1),
        (0, 2, 0), (1, 2, 0), (1, 2, 1),
    ]
    return [jnp.concatenate(g, axis=1) if len(g) > 1 else g[0] for g in groups], tags


def pick(blocks, index):
    return lax.dynamic_index_in_dim(blocks, index, axis=1, keepdims=False)


def reduce_rows(partial):
    width = partial.shape[1]
    core = lax.axis_index("core")
    halves = partial.reshape(16, 2, 32, width)
    kept = pick(halves, core) + lax.ppermute(pick(halves, 1 - core), "core", SWAP)
    kept = ring_reduce(kept.reshape(8, 64, width), "z")
    yh = lax.axis_index("yh")
    pairs = kept.reshape(2, 32, width)
    own = lax.dynamic_index_in_dim(pairs, yh, axis=0, keepdims=False)
    other = lax.dynamic_index_in_dim(pairs, 1 - yh, axis=0, keepdims=False)
    return own + lax.ppermute(other, "yh", SWAP)


def ring_reduce(blocks, axis):
    n = blocks.shape[0]
    me = lax.axis_index(axis)
    half = blocks.shape[2] // 2
    fwd, bwd = blocks[:, :, :half], blocks[:, :, half:]
    up = [(i, (i + 1) % n) for i in range(n)]
    down = [(i, (i - 1) % n) for i in range(n)]
    take = lambda b, k: lax.dynamic_index_in_dim(b, k % n, axis=0, keepdims=False)
    acc_f = take(fwd, me + n - 1)
    acc_b = take(bwd, me + 1)
    for step in range(n - 1):
        acc_f = lax.ppermute(acc_f, axis, up) + take(fwd, me + 2 * n - step - 2)
        acc_b = lax.ppermute(acc_b, axis, down) + take(bwd, me + step + 2)
    return jnp.concatenate([acc_f, acc_b], axis=1)


def per_device(factor, covariance, inv_diagonal, columns):
    groups, tags = gather_columns(covariance)
    product = jnp.concatenate([contract_rows(factor, g) for g in groups], axis=1)
    reduced = reduce_rows(product)
    rows = reduced.shape[0]
    place = {tag: k for k, tag in enumerate(tags)}
    order = [place[(dy, dx, half)] for dy in range(2) for dx in range(4) for half in range(2)]
    reduced = jnp.concatenate([reduced[:, k * 128:(k + 1) * 128] for k in order], axis=1)
    yl, x = lax.axis_index("yl"), lax.axis_index("x")
    blocks = reduced.reshape(rows, 2, 4, -1)
    blocks = jnp.where(yl == 1, blocks[:, ::-1], blocks)
    blocks = jnp.roll(blocks, x, axis=2)
    reduced = blocks.reshape(rows, -1)
    row_index = (lax.axis_index("z") * 2 + lax.axis_index("yh")) * 2 + lax.axis_index("core")
    block_index = (yl * 4 + x) * 32 + row_index
    row_ids = block_index * rows + lax.iota(jnp.int32, rows)
    on_diagonal = row_ids[:, None] == columns[None, :]
    return jnp.where(on_diagonal, inv_diagonal[:, None], jnp.zeros((), jnp.float32)) - reduced


def solution(mesh):
    devices = mesh.devices.reshape(8, 2, 2, 2, 4)
    fine = Mesh(devices, ("z", "yh", "core", "yl", "x"))
    return jax.shard_map(
        per_device,
        mesh=fine,
        in_specs=(P(ROW, COL), P(ROW, COL), P(COL + ROW), P()),
        out_specs=P(COL + ROW, None),
        check_vma=False,
    )
```

```python
import jax
import jax.numpy as jnp
from jax import lax
from jax.sharding import Mesh
from jax.sharding import PartitionSpec as P

ROW = ("z", "yh", "core")
COL = ("yl", "x")
SWAP = [(0, 1), (1, 0)]


def shift_x(step):
    return [(i, (i + step) % 4) for i in range(4)]


def contract_rows(left_block, right_block):
    return lax.dot_general(
        left_block,
        right_block,
        (((0,), (0,)), ((), ())),
        precision=lax.Precision.HIGHEST,
        preferred_element_type=jnp.float32,
    )


def gather_columns(cov):
    h0, h1 = cov[:, :128], cov[:, 128:]
    h0_y = lax.ppermute(h0, "yl", SWAP)
    h1_m = lax.ppermute(h1, "x", shift_x(1))
    h1_p = lax.ppermute(h1, "x", shift_x(-1))
    pair = jnp.concatenate([h0, h0_y], axis=1)
    pair_m = lax.ppermute(pair, "x", shift_x(1))
    pair_p = lax.ppermute(pair, "x", shift_x(-1))
    h1_fa = lax.ppermute(h1_m[:, :64], "x", shift_x(1))
    h1_fb = lax.ppermute(h1_p[:, 64:], "x", shift_x(-1))
    h1_y = lax.ppermute(jnp.concatenate([h1, h1_m, h1_p], axis=1), "yl", SWAP)
    pair_fa = lax.ppermute(pair_m[:, :128], "x", shift_x(1))
    pair_fb = lax.ppermute(pair_p[:, 128:], "x", shift_x(-1))
    h1_far = jnp.concatenate([h1_fa, h1_fb], axis=1)
    h1_far_y = lax.ppermute(h1_far, "yl", SWAP)
    groups = [
        [cov],
        [h0_y, h1_m, h1_p],
        [pair_m, pair_p, h1_far, h1_y],
        [pair_fa, pair_fb, h1_far_y],
    ]
    tags = [
        (0, 0, 0), (0, 0, 1),
        (1, 0, 0), (0, 3, 1), (0, 1, 1),
        (0, 3, 0), (1, 3, 0), (0, 1, 0), (1, 1, 0), (0, 2, 1), (1, 0, 1), (1, 3, 1), (1, 1, 1),
        (0, 2, 0), (1, 2, 0), (1, 2, 1),
    ]
    return [jnp.concatenate(g, axis=1) if len(g) > 1 else g[0] for g in groups], tags


def pick(blocks, index):
    return lax.dynamic_index_in_dim(blocks, index, axis=1, keepdims=False)


def reduce_rows(partial):
    width = partial.shape[1]
    kept = ring_reduce(partial.reshape(8, 64, width), "z")
    yh = lax.axis_index("yh")
    pairs = kept.reshape(2, 32, width)
    own = lax.dynamic_index_in_dim(pairs, yh, axis=0, keepdims=False)
    other = lax.dynamic_index_in_dim(pairs, 1 - yh, axis=0, keepdims=False)
    return own + lax.ppermute(other, "yh", SWAP)


def ring_reduce(blocks, axis):
    n = blocks.shape[0]
    me = lax.axis_index(axis)
    half = blocks.shape[2] // 2
    fwd, bwd = blocks[:, :, :half], blocks[:, :, half:]
    up = [(i, (i + 1) % n) for i in range(n)]
    down = [(i, (i - 1) % n) for i in range(n)]
    take = lambda b, k: lax.dynamic_index_in_dim(b, k % n, axis=0, keepdims=False)
    acc_f = take(fwd, me + n - 1)
    acc_b = take(bwd, me + 1)
    for step in range(n - 1):
        acc_f = lax.ppermute(acc_f, axis, up) + take(fwd, me + 2 * n - step - 2)
        acc_b = lax.ppermute(acc_b, axis, down) + take(bwd, me + step + 2)
    return jnp.concatenate([acc_f, acc_b], axis=1)


def per_device(factor, covariance, inv_diagonal, columns):
    groups, tags = gather_columns(covariance)
    core = lax.axis_index("core")
    by_core = factor.reshape(factor.shape[0], 16, 2, 32)
    own_cols = lax.dynamic_index_in_dim(by_core, core, axis=2, keepdims=False).reshape(factor.shape[0], -1)
    other_cols = lax.dynamic_index_in_dim(by_core, 1 - core, axis=2, keepdims=False).reshape(factor.shape[0], -1)
    received = [lax.ppermute(contract_rows(other_cols, g), "core", SWAP) for g in groups]
    kept = [contract_rows(own_cols, g) for g in groups]
    kept = jnp.concatenate(kept, axis=1) + jnp.concatenate(received, axis=1)
    reduced = reduce_rows(kept)
    rows = reduced.shape[0]
    place = {tag: k for k, tag in enumerate(tags)}
    order = [place[(dy, dx, half)] for dy in range(2) for dx in range(4) for half in range(2)]
    reduced = jnp.concatenate([reduced[:, k * 128:(k + 1) * 128] for k in order], axis=1)
    yl, x = lax.axis_index("yl"), lax.axis_index("x")
    blocks = reduced.reshape(rows, 2, 4, -1)
    blocks = jnp.where(yl == 1, blocks[:, ::-1], blocks)
    blocks = jnp.roll(blocks, x, axis=2)
    reduced = blocks.reshape(rows, -1)
    row_index = (lax.axis_index("z") * 2 + lax.axis_index("yh")) * 2 + lax.axis_index("core")
    block_index = (yl * 4 + x) * 32 + row_index
    row_ids = block_index * rows + lax.iota(jnp.int32, rows)
    on_diagonal = row_ids[:, None] == columns[None, :]
    return jnp.where(on_diagonal, inv_diagonal[:, None], jnp.zeros((), jnp.float32)) - reduced


def solution(mesh):
    devices = mesh.devices.reshape(8, 2, 2, 2, 4)
    fine = Mesh(devices, ("z", "yh", "core", "yl", "x"))
    return jax.shard_map(
        per_device,
        mesh=fine,
        in_specs=(P(ROW, COL), P(ROW, COL), P(COL + ROW), P()),
        out_specs=P(COL + ROW, None),
        check_vma=False,
    )
```

```python
import jax
import jax.numpy as jnp
from jax import lax
from jax.sharding import Mesh
from jax.sharding import PartitionSpec as P

ROW = ("z", "yh", "core")
COL = ("yl", "x")
SWAP = [(0, 1), (1, 0)]


def shift_x(step):
    return [(i, (i + step) % 4) for i in range(4)]


def contract_rows(left_block, right_block):
    return lax.dot_general(
        left_block,
        right_block,
        (((0,), (0,)), ((), ())),
        precision=lax.Precision.HIGHEST,
        preferred_element_type=jnp.float32,
    )


def gather_columns(cov):
    h0, h1 = cov[:, :128], cov[:, 128:]
    h0_y = lax.ppermute(h0, "yl", SWAP)
    h1_m = lax.ppermute(h1, "x", shift_x(1))
    h1_p = lax.ppermute(h1, "x", shift_x(-1))
    pair = jnp.concatenate([h0, h0_y], axis=1)
    pair_m = lax.ppermute(pair, "x", shift_x(1))
    pair_p = lax.ppermute(pair, "x", shift_x(-1))
    h1_fa = lax.ppermute(h1_m[:, :64], "x", shift_x(1))
    h1_fb = lax.ppermute(h1_p[:, 64:], "x", shift_x(-1))
    h1_y = lax.ppermute(jnp.concatenate([h1, h1_m, h1_p], axis=1), "yl", SWAP)
    pair_fa = lax.ppermute(pair_m[:, :128], "x", shift_x(1))
    pair_fb = lax.ppermute(pair_p[:, 128:], "x", shift_x(-1))
    h1_far = jnp.concatenate([h1_fa, h1_fb], axis=1)
    h1_far_y = lax.ppermute(h1_far, "yl", SWAP)
    groups = [
        [cov],
        [h0_y, h1_m, h1_p],
        [pair_m, pair_p, h1_far, h1_y],
        [pair_fa, pair_fb, h1_far_y],
    ]
    tags = [
        (0, 0, 0), (0, 0, 1),
        (1, 0, 0), (0, 3, 1), (0, 1, 1),
        (0, 3, 0), (1, 3, 0), (0, 1, 0), (1, 1, 0), (0, 2, 1), (1, 0, 1), (1, 3, 1), (1, 1, 1),
        (0, 2, 0), (1, 2, 0), (1, 2, 1),
    ]
    return [jnp.concatenate(g, axis=1) if len(g) > 1 else g[0] for g in groups], tags


def pick(blocks, index):
    return lax.dynamic_index_in_dim(blocks, index, axis=1, keepdims=False)


def reduce_rows(partial):
    width = partial.shape[1]
    kept = ring_reduce(partial.reshape(8, 64, width), "z")
    yh = lax.axis_index("yh")
    pairs = kept.reshape(2, 32, width)
    own = lax.dynamic_index_in_dim(pairs, yh, axis=0, keepdims=False)
    other = lax.dynamic_index_in_dim(pairs, 1 - yh, axis=0, keepdims=False)
    return own + lax.ppermute(other, "yh", SWAP)


def ring_reduce(blocks, axis):
    n = blocks.shape[0]
    me = lax.axis_index(axis)
    half = blocks.shape[2] // 2
    fwd, bwd = blocks[:, :, :half], blocks[:, :, half:]
    up = [(i, (i + 1) % n) for i in range(n)]
    down = [(i, (i - 1) % n) for i in range(n)]
    take = lambda b, k: lax.dynamic_index_in_dim(b, k % n, axis=0, keepdims=False)
    acc_f = take(fwd, me + n - 1)
    acc_b = take(bwd, me + 1)
    def step(k, accs):
        acc_f, acc_b = accs
        acc_f = lax.ppermute(acc_f, axis, up) + take(fwd, me + 2 * n - k - 2)
        acc_b = lax.ppermute(acc_b, axis, down) + take(bwd, me + k + 2)
        return acc_f, acc_b

    acc_f, acc_b = lax.fori_loop(0, n - 1, step, (acc_f, acc_b))
    return jnp.concatenate([acc_f, acc_b], axis=1)


def per_device(factor, covariance, inv_diagonal, columns):
    groups, tags = gather_columns(covariance)
    core = lax.axis_index("core")
    by_core = factor.reshape(factor.shape[0], 16, 2, 32)
    own_cols = lax.dynamic_index_in_dim(by_core, core, axis=2, keepdims=False).reshape(factor.shape[0], -1)
    other_cols = lax.dynamic_index_in_dim(by_core, 1 - core, axis=2, keepdims=False).reshape(factor.shape[0], -1)
    received = [lax.ppermute(contract_rows(other_cols, g), "core", SWAP) for g in groups]
    kept = [contract_rows(own_cols, g) for g in groups]
    kept = jnp.concatenate(kept, axis=1) + jnp.concatenate(received, axis=1)
    reduced = reduce_rows(kept)
    rows = reduced.shape[0]
    place = {tag: k for k, tag in enumerate(tags)}
    order = [place[(dy, dx, half)] for dy in range(2) for dx in range(4) for half in range(2)]
    reduced = jnp.concatenate([reduced[:, k * 128:(k + 1) * 128] for k in order], axis=1)
    yl, x = lax.axis_index("yl"), lax.axis_index("x")
    blocks = reduced.reshape(rows, 2, 4, -1)
    blocks = jnp.where(yl == 1, blocks[:, ::-1], blocks)
    blocks = jnp.roll(blocks, x, axis=2)
    reduced = blocks.reshape(rows, -1)
    row_index = (lax.axis_index("z") * 2 + lax.axis_index("yh")) * 2 + lax.axis_index("core")
    block_index = (yl * 4 + x) * 32 + row_index
    row_ids = block_index * rows + lax.iota(jnp.int32, rows)
    on_diagonal = row_ids[:, None] == columns[None, :]
    return jnp.where(on_diagonal, inv_diagonal[:, None], jnp.zeros((), jnp.float32)) - reduced


def solution(mesh):
    devices = mesh.devices.reshape(8, 2, 2, 2, 4)
    fine = Mesh(devices, ("z", "yh", "core", "yl", "x"))
    return jax.shard_map(
        per_device,
        mesh=fine,
        in_specs=(P(ROW, COL), P(ROW, COL), P(COL + ROW), P()),
        out_specs=P(COL + ROW, None),
        check_vma=False,
    )
```

```python
import jax
import jax.numpy as jnp
from jax import lax
from jax.sharding import Mesh
from jax.sharding import PartitionSpec as P

ROW = ("z", "yh", "core")
COL = ("yl", "x")
SWAP = [(0, 1), (1, 0)]


def shift_x(step):
    return [(i, (i + step) % 4) for i in range(4)]


def contract_rows(left_block, right_block):
    return lax.dot_general(
        left_block,
        right_block,
        (((0,), (0,)), ((), ())),
        precision=lax.Precision.HIGH,
        preferred_element_type=jnp.float32,
    )


def gather_columns(cov):
    h0, h1 = cov[:, :128], cov[:, 128:]
    h0_y = lax.ppermute(h0, "yl", SWAP)
    h1_m = lax.ppermute(h1, "x", shift_x(1))
    h1_p = lax.ppermute(h1, "x", shift_x(-1))
    pair = jnp.concatenate([h0, h0_y], axis=1)
    pair_m = lax.ppermute(pair, "x", shift_x(1))
    pair_p = lax.ppermute(pair, "x", shift_x(-1))
    h1_fa = lax.ppermute(h1_m[:, :64], "x", shift_x(1))
    h1_fb = lax.ppermute(h1_p[:, 64:], "x", shift_x(-1))
    h1_y = lax.ppermute(jnp.concatenate([h1, h1_m, h1_p], axis=1), "yl", SWAP)
    pair_fa = lax.ppermute(pair_m[:, :128], "x", shift_x(1))
    pair_fb = lax.ppermute(pair_p[:, 128:], "x", shift_x(-1))
    h1_far = jnp.concatenate([h1_fa, h1_fb], axis=1)
    h1_far_y = lax.ppermute(h1_far, "yl", SWAP)
    groups = [
        [cov],
        [h0_y, h1_m, h1_p],
        [pair_m, pair_p, h1_far, h1_y],
        [pair_fa, pair_fb, h1_far_y],
    ]
    tags = [
        (0, 0, 0), (0, 0, 1),
        (1, 0, 0), (0, 3, 1), (0, 1, 1),
        (0, 3, 0), (1, 3, 0), (0, 1, 0), (1, 1, 0), (0, 2, 1), (1, 0, 1), (1, 3, 1), (1, 1, 1),
        (0, 2, 0), (1, 2, 0), (1, 2, 1),
    ]
    return [jnp.concatenate(g, axis=1) if len(g) > 1 else g[0] for g in groups], tags


def pick(blocks, index):
    return lax.dynamic_index_in_dim(blocks, index, axis=1, keepdims=False)


def reduce_rows(partial):
    width = partial.shape[1]
    kept = ring_reduce(partial.reshape(8, 64, width), "z")
    yh = lax.axis_index("yh")
    pairs = kept.reshape(2, 32, width)
    own = lax.dynamic_index_in_dim(pairs, yh, axis=0, keepdims=False)
    other = lax.dynamic_index_in_dim(pairs, 1 - yh, axis=0, keepdims=False)
    return own + lax.ppermute(other, "yh", SWAP)


def ring_reduce(blocks, axis):
    n = blocks.shape[0]
    me = lax.axis_index(axis)
    half = blocks.shape[2] // 2
    fwd, bwd = blocks[:, :, :half], blocks[:, :, half:]
    up = [(i, (i + 1) % n) for i in range(n)]
    down = [(i, (i - 1) % n) for i in range(n)]
    take = lambda b, k: lax.dynamic_index_in_dim(b, k % n, axis=0, keepdims=False)
    acc_f = take(fwd, me + n - 1)
    acc_b = take(bwd, me + 1)
    for step in range(n - 1):
        acc_f = lax.ppermute(acc_f, axis, up) + take(fwd, me + 2 * n - step - 2)
        acc_b = lax.ppermute(acc_b, axis, down) + take(bwd, me + step + 2)
    return jnp.concatenate([acc_f, acc_b], axis=1)


def per_device(factor, covariance, inv_diagonal, columns):
    groups, tags = gather_columns(covariance)
    core = lax.axis_index("core")
    by_core = factor.reshape(factor.shape[0], 16, 2, 32)
    own_cols = lax.dynamic_index_in_dim(by_core, core, axis=2, keepdims=False).reshape(factor.shape[0], -1)
    other_cols = lax.dynamic_index_in_dim(by_core, 1 - core, axis=2, keepdims=False).reshape(factor.shape[0], -1)
    received = [lax.ppermute(contract_rows(other_cols, g), "core", SWAP) for g in groups]
    kept = [contract_rows(own_cols, g) for g in groups]
    kept = jnp.concatenate(kept, axis=1) + jnp.concatenate(received, axis=1)
    reduced = reduce_rows(kept)
    rows = reduced.shape[0]
    place = {tag: k for k, tag in enumerate(tags)}
    order = [place[(dy, dx, half)] for dy in range(2) for dx in range(4) for half in range(2)]
    reduced = jnp.concatenate([reduced[:, k * 128:(k + 1) * 128] for k in order], axis=1)
    yl, x = lax.axis_index("yl"), lax.axis_index("x")
    blocks = reduced.reshape(rows, 2, 4, -1)
    blocks = jnp.where(yl == 1, blocks[:, ::-1], blocks)
    blocks = jnp.roll(blocks, x, axis=2)
    reduced = blocks.reshape(rows, -1)
    row_index = (lax.axis_index("z") * 2 + lax.axis_index("yh")) * 2 + lax.axis_index("core")
    block_index = (yl * 4 + x) * 32 + row_index
    row_ids = block_index * rows + lax.iota(jnp.int32, rows)
    on_diagonal = row_ids[:, None] == columns[None, :]
    return jnp.where(on_diagonal, inv_diagonal[:, None], jnp.zeros((), jnp.float32)) - reduced


def solution(mesh):
    devices = mesh.devices.reshape(8, 2, 2, 2, 4)
    fine = Mesh(devices, ("z", "yh", "core", "yl", "x"))
    return jax.shard_map(
        per_device,
        mesh=fine,
        in_specs=(P(ROW, COL), P(ROW, COL), P(COL + ROW), P()),
        out_specs=P(COL + ROW, None),
        check_vma=False,
    )
```

```python
import jax
import jax.numpy as jnp
from jax import lax
from jax.sharding import Mesh
from jax.sharding import PartitionSpec as P

ROW = ("z", "yh", "core")
COL = ("yl", "x")
SWAP = [(0, 1), (1, 0)]


def shift_x(step):
    return [(i, (i + step) % 4) for i in range(4)]


def contract_rows(left_block, right_block):
    return lax.dot_general(
        left_block,
        right_block,
        (((0,), (0,)), ((), ())),
        precision=lax.Precision.HIGHEST,
        preferred_element_type=jnp.float32,
    )


def gather_columns(cov):
    h0, h1 = cov[:, :128], cov[:, 128:]
    h0_y = lax.ppermute(h0, "yl", SWAP)
    h1_m = lax.ppermute(h1, "x", shift_x(1))
    h1_p = lax.ppermute(h1, "x", shift_x(-1))
    pair = jnp.concatenate([h0, h0_y], axis=1)
    pair_m = lax.ppermute(pair, "x", shift_x(1))
    pair_p = lax.ppermute(pair, "x", shift_x(-1))
    h1_fa = lax.ppermute(h1_m[:, :64], "x", shift_x(1))
    h1_fb = lax.ppermute(h1_p[:, 64:], "x", shift_x(-1))
    h1_y = lax.ppermute(jnp.concatenate([h1, h1_m, h1_p], axis=1), "yl", SWAP)
    pair_fa = lax.ppermute(pair_m[:, :128], "x", shift_x(1))
    pair_fb = lax.ppermute(pair_p[:, 128:], "x", shift_x(-1))
    h1_far = jnp.concatenate([h1_fa, h1_fb], axis=1)
    h1_far_y = lax.ppermute(h1_far, "yl", SWAP)
    groups = [
        [cov],
        [h0_y, h1_m, h1_p],
        [pair_m, pair_p, h1_far, h1_y],
        [pair_fa, pair_fb, h1_far_y],
    ]
    tags = [
        (0, 0, 0), (0, 0, 1),
        (1, 0, 0), (0, 3, 1), (0, 1, 1),
        (0, 3, 0), (1, 3, 0), (0, 1, 0), (1, 1, 0), (0, 2, 1), (1, 0, 1), (1, 3, 1), (1, 1, 1),
        (0, 2, 0), (1, 2, 0), (1, 2, 1),
    ]
    return [jnp.concatenate(g, axis=1) if len(g) > 1 else g[0] for g in groups], tags


def pick(blocks, index):
    return lax.dynamic_index_in_dim(blocks, index, axis=1, keepdims=False)


def reduce_rows(partial):
    kept = ring_reduce(partial[0], partial[1], "z")
    width = kept.shape[1]
    yh = lax.axis_index("yh")
    pairs = kept.reshape(2, 32, width)
    own = lax.dynamic_index_in_dim(pairs, yh, axis=0, keepdims=False)
    other = lax.dynamic_index_in_dim(pairs, 1 - yh, axis=0, keepdims=False)
    return own + lax.ppermute(other, "yh", SWAP)


def ring_reduce(fwd, bwd, axis):
    n = fwd.shape[0]
    me = lax.axis_index(axis)
    up = [(i, (i + 1) % n) for i in range(n)]
    down = [(i, (i - 1) % n) for i in range(n)]
    take = lambda b, k: lax.dynamic_index_in_dim(b, k % n, axis=0, keepdims=False)
    acc_f = take(fwd, me + n - 1)
    acc_b = take(bwd, me + 1)
    for step in range(n - 1):
        acc_f = lax.ppermute(acc_f, axis, up) + take(fwd, me + 2 * n - step - 2)
        acc_b = lax.ppermute(acc_b, axis, down) + take(bwd, me + step + 2)
    return jnp.concatenate([acc_f, acc_b], axis=1)


def per_device(factor, covariance, inv_diagonal, columns):
    groups, tags = gather_columns(covariance)
    core = lax.axis_index("core")
    by_core = factor.reshape(factor.shape[0], 16, 2, 32)
    own_cols = lax.dynamic_index_in_dim(by_core, core, axis=2, keepdims=False).reshape(factor.shape[0], -1)
    other_cols = lax.dynamic_index_in_dim(by_core, 1 - core, axis=2, keepdims=False).reshape(factor.shape[0], -1)
    received = [lax.ppermute(contract_rows(other_cols, g), "core", SWAP) for g in groups]
    kept = [contract_rows(own_cols, g) for g in groups]
    half = covariance.shape[1] * 4
    halves = []
    for lo in (0, half):
        parts, start = [], 0
        for k, r in zip(kept, received):
            width = k.shape[1]
            a, b = max(lo, start), min(lo + half, start + width)
            if a < b:
                parts.append(k[:, a - start:b - start] + r[:, a - start:b - start])
            start += width
        halves.append(jnp.concatenate(parts, axis=1).reshape(8, 64, half))
    reduced = reduce_rows(halves)
    rows = reduced.shape[0]
    place = {tag: k for k, tag in enumerate(tags)}
    order = [place[(dy, dx, half)] for dy in range(2) for dx in range(4) for half in range(2)]
    reduced = jnp.concatenate([reduced[:, k * 128:(k + 1) * 128] for k in order], axis=1)
    yl, x = lax.axis_index("yl"), lax.axis_index("x")
    blocks = reduced.reshape(rows, 2, 4, -1)
    blocks = jnp.where(yl == 1, blocks[:, ::-1], blocks)
    blocks = jnp.roll(blocks, x, axis=2)
    reduced = blocks.reshape(rows, -1)
    row_index = (lax.axis_index("z") * 2 + lax.axis_index("yh")) * 2 + lax.axis_index("core")
    block_index = (yl * 4 + x) * 32 + row_index
    row_ids = block_index * rows + lax.iota(jnp.int32, rows)
    on_diagonal = row_ids[:, None] == columns[None, :]
    return jnp.where(on_diagonal, inv_diagonal[:, None], jnp.zeros((), jnp.float32)) - reduced


def solution(mesh):
    devices = mesh.devices.reshape(8, 2, 2, 2, 4)
    fine = Mesh(devices, ("z", "yh", "core", "yl", "x"))
    return jax.shard_map(
        per_device,
        mesh=fine,
        in_specs=(P(ROW, COL), P(ROW, COL), P(COL + ROW), P()),
        out_specs=P(COL + ROW, None),
        check_vma=False,
    )
```
